256 devices in a mesh: dp: 16 (over z, core), row: 4 (over x), col: 4 (over y).
Axes of the slice: x: 4, y: 4, z: 8, core: 2. Of those that a mesh axis runs over, the one named last changes fastest.
Arguments:
- latent: bfloat16 [16, 32, 64, 768], P('dp', 'row', 'col'), may hold values from -6 to 6
- norm_shift: float32 [16, 768], P('dp'), may hold values from -3 to 3
- norm_scale: float32 [16, 768], P('dp'), may hold values from -3 to 3
- branch_gate: float32 [16, 768], P('dp'), may hold values from -4 to 4
- query_key_value: bfloat16 [768, 2304], replicated, may hold values from -0.21875 to 0.21875
- output_weight: bfloat16 [768, 768], replicated, may hold values from -0.21875 to 0.21875
- tile_valid: int32 [16, 4, 8], P('dp'), may hold values from 0 to 1, as said below
- cotangent: bfloat16 [16, 32, 64, 768], P('dp', 'row', 'col'), may hold values from -6 to 6
Outputs:
- block_output: bfloat16 [16, 32, 64, 768], P('dp', 'row', 'col')
- latent_gradient: bfloat16 [16, 32, 64, 768], P('dp', 'row', 'col')
- projection_gradient: float32 [768, 2304], P('dp', ('row', 'col'))
- output_weight_gradient: float32 [768, 768], P('dp', ('row', 'col'))
- shift_gradient: float32 [16, 768], P('dp')
- scale_gradient: float32 [16, 768], P('dp')
- gate_gradient: float32 [16, 768], P('dp')
The draws below stay inside these ranges and needn't reach their ends.
Inputs may be any that keep to these rules, and one draw needn't show every extreme that they name: `tile_valid`: the valid tiles of each sample form a rectangle that starts at tile (0, 0), at least 2 tiles tall and 3 tiles wide; sample 0 is exactly 2 tiles tall.
All inputs are finite; a program needn't handle non-finite values.
Results may differ from the reference program's by a relative error of at most 0.02.
Values may be sent and summed in bfloat16 or wider, within the bound.
No kernel may reach another device: no remote copies, remote signals or barrier semaphores. Data moves between devices by JAX's collectives and lax.ppermute only.
A program may use at most 128 MiB of HBM per device.

```python
import math
import jax
import jax.numpy as jnp
from jax import lax

HEAD_DIM = 64
D = 768
TILE = 8
TR = 1
TC = 2
BATCH = 16
NTR = 4
NTC = 8
IMG_R = 32
IMG_C = 64


def draw_tile_valid(key, part):
    key_tall = jax.random.fold_in(key, 11)
    key_wide = jax.random.fold_in(key, 23)
    heights = jax.random.randint(key_tall, (BATCH,), TR + 1, NTR + 1)
    widths = jax.random.randint(key_wide, (BATCH,), TC + 1, NTC + 1)
    heights = heights.at[0].set(TR + 1)
    row_index = jnp.arange(NTR, dtype=jnp.int32)[None, :, None]
    col_index = jnp.arange(NTC, dtype=jnp.int32)[None, None, :]
    inside = (row_index < heights[:, None, None]) & (col_index < widths[:, None, None])
    return inside.astype(jnp.int32)


def with_spikes(values, stream_key, source, target, parts, factor):
    def block_of(axis_at):
        return (jnp.arange(values.shape[axis_at]) // (values.shape[axis_at] // parts)).reshape((-1,) + (1,) * (values.ndim - 1 - axis_at))

    first = jax.random.permutation(stream_key, parts)[block_of(target)]
    other_side = (block_of(target) + parts // 2) % parts
    return jnp.where((block_of(source) == first) | (block_of(source) == other_side), factor * values, values)


def block_levels(own_key, extent, split, least, top_value):
    level, own = 1.0, jax.random.fold_in(own_key, 6)
    for dim, shards_of in split:
        steps = jnp.exp(jax.random.uniform(jax.random.fold_in(own, dim), (shards_of,), jnp.float32, least / len(split), top_value / len(split)))
        level = level * jnp.repeat(steps, extent[dim] // shards_of).reshape([-1 if axis == dim else 1 for axis in range(len(extent))])
    return level


def scatter_about(own_key, extent, scale, bound, cuts=(), kind=jnp.bfloat16):
    values = jax.random.normal(own_key, extent, jnp.float32) * scale
    if len(cuts) > 0:
        values = block_levels(own_key, extent, cuts, -0.22, 0.18) * values
    return jnp.clip(values, min=-bound, max=bound).astype(kind)


def heavy_noise(rng, shape, spread, bound, cuts, heavy, held_as=jnp.bfloat16):
    result = spread * jax.random.normal(rng, shape, jnp.float32)
    if cuts:
        result = result * block_levels(rng, shape, cuts, -0.22, 0.18)
    return jnp.clip(with_spikes(result, jax.random.fold_in(rng, 3), *heavy), -bound, bound).astype(held_as)


def setup_inputs(seed: int = 0) -> dict:
    arg_keys = jax.random.split(jax.random.key(seed), 9)
    latent = scatter_about(arg_keys[0], (BATCH, IMG_R, IMG_C, D), 1.0, 6.0, ((0, 16), (1, 4), (2, 4)))
    norm_shift = scatter_about(arg_keys[1], (BATCH, D), 0.5, 3.0, ((0, 16),), jnp.float32)
    norm_scale = scatter_about(arg_keys[2], (BATCH, D), 0.5, 3.0, ((0, 16),), jnp.float32)
    branch_gate = scatter_about(arg_keys[3], (BATCH, D), 1.0, 4.0, ((0, 16),), jnp.float32)
    query_key_value = scatter_about(arg_keys[4], (D, 3 * D), D ** -0.5, 0.21875)
    output_weight = scatter_about(arg_keys[5], (D, D), D ** -0.5, 0.21875)
    tile_valid = draw_tile_valid(jax.random.fold_in(arg_keys[8], 71), 0)
    cotangent = heavy_noise(arg_keys[7], (BATCH, IMG_R, IMG_C, D), 1.0, 6.0, ((0, 16), (1, 4), (2, 4)), (0, 3, 16, 2.0))
    return {"latent": latent, "norm_shift": norm_shift, "norm_scale": norm_scale, "branch_gate": branch_gate, "query_key_value": query_key_value, "output_weight": output_weight, "tile_valid": tile_valid, "cotangent": cotangent}


EPSILON = 1e-06

def product(form, left, right):
    return jnp.einsum(form, left.astype(jnp.float32), right.astype(jnp.float32))

def to_tiles(latent_image):
    samples, height, across, features = latent_image.shape
    blocks = latent_image.reshape(samples, height // TILE, TILE, across // TILE, TILE, features)
    blocks = blocks.transpose(0, 1, 3, 2, 4, 5)
    return blocks.reshape(samples, height // TILE, across // TILE, TILE * TILE, features)

def from_tiles(tiled):
    samples, tile_rows, tile_cols, tile_cells, features = tiled.shape
    blocks = tiled.reshape(samples, tile_rows, tile_cols, TILE, TILE, features)
    blocks = blocks.transpose(0, 1, 3, 2, 4, 5)
    return blocks.reshape(samples, tile_rows * TILE, tile_cols * TILE, features)

def neighbours(padded):
    tile_rows = padded.shape[1] - 2
    tile_cols = padded.shape[2] - 2
    shifted = [padded[:, offset_row:offset_row + tile_rows, offset_col:offset_col + tile_cols] for offset_row in range(3) for offset_col in range(3)]
    return jnp.concatenate(shifted, axis=3)

def spread_back(gathered):
    samples, tile_rows, tile_cols, key_count, features = gathered.shape
    tile_cells = key_count // 9
    accumulated = jnp.zeros((samples, tile_rows + 2, tile_cols + 2, tile_cells, features), jnp.float32)
    for position in range(9):
        offset_row = position // 3
        offset_col = position % 3
        section = gathered[:, :, :, position * tile_cells:(position + 1) * tile_cells]
        accumulated = accumulated + jnp.pad(section, ((0, 0), (offset_row, 2 - offset_row), (offset_col, 2 - offset_col), (0, 0), (0, 0)))
    return accumulated

def front(latent, norm_shift, norm_scale, weight):
    values = latent.astype(jnp.float32)
    center = values - lax.optimization_barrier(jnp.mean(values, axis=-1, keepdims=True))
    inverse = lax.rsqrt(lax.optimization_barrier(jnp.mean(center * center, axis=-1, keepdims=True)) + EPSILON)
    normed = center * inverse
    modulated = (normed * (1.0 + norm_scale[:, None, None, :]) + norm_shift[:, None, None, :]).astype(jnp.bfloat16)
    samples, height, across, model_width = latent.shape
    mixing = jnp.dot(modulated.reshape(-1, model_width), weight, preferred_element_type=jnp.float32)
    projections = mixing.astype(jnp.bfloat16).reshape(samples, height, across, 3 * model_width)
    return (normed, inverse, modulated, projections)

def attend(queries, keys_nine, values_nine, key_valid, query_valid):
    scores = product('srcqhe,srckhe->srchqk', queries, keys_nine) * (1.0 / math.sqrt(HEAD_DIM))
    unnormed = jnp.exp(scores) * key_valid[:, :, :, None, None, :]
    denominator = lax.optimization_barrier(jnp.sum(unnormed, axis=-1, keepdims=True)) + (1.0 - query_valid)[:, :, :, None, None, None]
    attention = (unnormed / denominator).astype(jnp.bfloat16)
    attended = product('srchqk,srckhe->srcqhe', attention, values_nine) * query_valid[:, :, :, None, None, None]
    return (attention, attended.astype(jnp.bfloat16))

def attend_back(queries, keys_nine, values_nine, attention, grad_attended):
    grad_weights = product('srcqhe,srckhe->srchqk', grad_attended, values_nine)
    attention_wide = attention.astype(jnp.float32)
    row_inner = lax.optimization_barrier(jnp.sum(attention_wide * grad_weights, axis=-1, keepdims=True))
    grad_scores = (attention_wide * (grad_weights - row_inner) * (1.0 / math.sqrt(HEAD_DIM))).astype(jnp.bfloat16)
    grad_queries = product('srchqk,srckhe->srcqhe', grad_scores, keys_nine).astype(jnp.bfloat16)
    grad_keys = product('srchqk,srcqhe->srckhe', grad_scores, queries)
    grad_values = product('srchqk,srcqhe->srckhe', attention, grad_attended)
    return (grad_queries, grad_keys, grad_values)

def branch_core(projections, kv_padded, mask_pad, branch_gate, cotangent, output_weight):
    samples, height, across, triple = projections.shape
    model_width = triple // 3
    head_count = model_width // HEAD_DIM
    tile_rows = height // TILE
    tile_cols = across // TILE
    tile_cells = TILE * TILE
    queries = to_tiles(projections[..., :model_width]).reshape(samples, tile_rows, tile_cols, tile_cells, head_count, HEAD_DIM)
    gathered = neighbours(to_tiles(kv_padded))
    keys_nine = gathered[..., :model_width].reshape(samples, tile_rows, tile_cols, 9 * tile_cells, head_count, HEAD_DIM)
    values_nine = gathered[..., model_width:].reshape(samples, tile_rows, tile_cols, 9 * tile_cells, head_count, HEAD_DIM)
    cell_mask = jnp.broadcast_to(mask_pad[:, :, :, None, None], mask_pad.shape + (tile_cells, 1))
    key_valid = neighbours(cell_mask)[..., 0]
    query_valid = mask_pad[:, 1:-1, 1:-1]
    attention, attended = attend(queries, keys_nine, values_nine, key_valid, query_valid)
    attended_image = from_tiles(attended.reshape(samples, tile_rows, tile_cols, tile_cells, model_width))
    flat_attended = attended_image.reshape(-1, model_width)
    projected = jnp.dot(flat_attended, output_weight, preferred_element_type=jnp.float32).reshape(samples, height, across, model_width)
    incoming = cotangent.astype(jnp.float32)
    gate_term = lax.optimization_barrier(jnp.sum(incoming * projected, axis=(1, 2)))
    grad_projected = (incoming * branch_gate[:, None, None, :]).astype(jnp.bfloat16)
    flat_grad = grad_projected.reshape(-1, model_width)
    output_term = product('nd,nf->df', flat_attended, flat_grad)
    grad_image = product('nf,df->nd', flat_grad, output_weight).reshape(samples, height, across, model_width)
    grad_attended = (to_tiles(grad_image) * query_valid[:, :, :, None, None]).astype(jnp.bfloat16)
    grad_attended = grad_attended.reshape(samples, tile_rows, tile_cols, tile_cells, head_count, HEAD_DIM)
    grad_queries, grad_keys, grad_values = attend_back(queries, keys_nine, values_nine, attention, grad_attended)
    query_image = from_tiles(grad_queries.reshape(samples, tile_rows, tile_cols, tile_cells, model_width))
    key_spread = spread_back(grad_keys.reshape(samples, tile_rows, tile_cols, 9 * tile_cells, model_width))
    value_spread = spread_back(grad_values.reshape(samples, tile_rows, tile_cols, 9 * tile_cells, model_width))
    pair_grads = from_tiles(jnp.concatenate([key_spread, value_spread], axis=-1))
    return (projected, gate_term, output_term, query_image, pair_grads)

def branch_back(query_image, pair_grads, modulated, normed, inverse, norm_scale, weight):
    samples, height, across, model_width = normed.shape
    grad_all = jnp.concatenate([query_image, pair_grads.astype(jnp.bfloat16)], axis=-1)
    flat_grad = grad_all.reshape(-1, 3 * model_width)
    input_term = product('nd,nf->df', modulated.reshape(-1, model_width), flat_grad)
    grad_modulated = product('nf,df->nd', flat_grad, weight).reshape(samples, height, across, model_width)
    shift_term = lax.optimization_barrier(jnp.sum(grad_modulated, axis=(1, 2)))
    scale_term = lax.optimization_barrier(jnp.sum(grad_modulated * normed, axis=(1, 2)))
    grad_normed = grad_modulated * (1.0 + norm_scale[:, None, None, :])
    latent_term = inverse * (grad_normed - lax.optimization_barrier(jnp.mean(grad_normed, axis=-1, keepdims=True)) - normed * lax.optimization_barrier(jnp.mean(grad_normed * normed, axis=-1, keepdims=True)))
    return (input_term, shift_term, scale_term, latent_term)

def reference(latent, norm_shift, norm_scale, branch_gate, query_key_value, output_weight, tile_valid, cotangent):
    model_width = latent.shape[-1]

    def one_sample(entries):
        latent_one, shift_one, scale_one, gate_one, valid_one, incoming_one = [element[None] for element in entries]
        normed, inverse, modulated, projections = front(latent_one, shift_one, scale_one, query_key_value)
        kv_padded = jnp.pad(projections[..., model_width:], ((0, 0), (TILE, TILE), (TILE, TILE), (0, 0)))
        mask_pad = jnp.pad(valid_one.astype(jnp.float32), ((0, 0), (1, 1), (1, 1)))
        projected, gate_term, output_term, query_image, pair_grads = branch_core(projections, kv_padded, mask_pad, gate_one, incoming_one, output_weight)
        pair_grads = pair_grads[:, TILE:-TILE, TILE:-TILE]
        input_term, shift_term, scale_term, latent_term = branch_back(query_image, pair_grads, modulated, normed, inverse, scale_one, query_key_value)
        mixed = (latent_one.astype(jnp.float32) + gate_one[:, None, None, :] * projected).astype(jnp.bfloat16)
        latent_grad = (incoming_one.astype(jnp.float32) + latent_term).astype(jnp.bfloat16)
        return (mixed[0], latent_grad[0], input_term, output_term, shift_term[0], scale_term[0], gate_term[0])
    results = lax.map(one_sample, (latent, norm_shift, norm_scale, branch_gate, tile_valid, cotangent))
    return (results[0], results[1], lax.optimization_barrier(jnp.sum(results[2], axis=0)), lax.optimization_barrier(jnp.sum(results[3], axis=0)), results[4], results[5], results[6])
```

```python
import math

import jax
import jax.numpy as jnp
import numpy as np
from jax import lax
from jax.sharding import PartitionSpec as P

HEAD_DIM = 64
TILE = 8
CELLS = TILE * TILE
EPSILON = 1e-06
F32 = jnp.float32
BF16 = jnp.bfloat16


def to_tiles(image):
    rows, cols, features = image.shape
    blocks = image.reshape(rows // TILE, TILE, cols // TILE, TILE, features)
    blocks = blocks.transpose(0, 2, 1, 3, 4)
    return blocks.reshape((rows // TILE) * (cols // TILE) * CELLS, features)


def from_tiles(flat, rows, cols):
    features = flat.shape[-1]
    blocks = flat.reshape(rows // TILE, cols // TILE, TILE, TILE, features)
    blocks = blocks.transpose(0, 2, 1, 3, 4)
    return blocks.reshape(rows, cols, features)


def forward_pairs(count):
    return [(i, i + 1) for i in range(count - 1)]


def backward_pairs(count):
    return [(i + 1, i) for i in range(count - 1)]


def halo(grid):
    rows, cols = lax.axis_size("row"), lax.axis_size("col")
    from_above = lax.ppermute(grid[-1:], "row", forward_pairs(rows))
    from_below = lax.ppermute(grid[:1], "row", backward_pairs(rows))
    grid = jnp.concatenate([from_above, grid, from_below], axis=0)
    from_left = lax.ppermute(grid[:, -1:], "col", forward_pairs(cols))
    from_right = lax.ppermute(grid[:, :1], "col", backward_pairs(cols))
    return jnp.concatenate([from_left, grid, from_right], axis=1)


def return_rims(grid):
    rows, cols = lax.axis_size("row"), lax.axis_size("col")
    tile_rows, tile_cols = grid.shape[0] - 2, grid.shape[1] - 2
    from_right = lax.ppermute(grid[:, :1].astype(BF16), "col", backward_pairs(cols))
    from_left = lax.ppermute(grid[:, -1:].astype(BF16), "col", forward_pairs(cols))
    middle = grid[:, 1:-1]
    pad_c = ((0, 0), (0, tile_cols - 1), (0, 0), (0, 0))
    middle = middle + jnp.pad(from_left.astype(F32), pad_c)
    middle = middle + jnp.pad(from_right.astype(F32), (pad_c[0], pad_c[1][::-1], pad_c[2], pad_c[3]))
    from_below = lax.ppermute(middle[:1].astype(BF16), "row", backward_pairs(rows))
    from_above = lax.ppermute(middle[-1:].astype(BF16), "row", forward_pairs(rows))
    inner = middle[1:-1]
    pad_r = ((0, tile_rows - 1), (0, 0), (0, 0), (0, 0))
    inner = inner + jnp.pad(from_above.astype(F32), pad_r)
    inner = inner + jnp.pad(from_below.astype(F32), (pad_r[0][::-1], pad_r[1], pad_r[2], pad_r[3]))
    return inner


def neighbour_table(tile_rows, tile_cols):
    grid_cols = tile_cols + 2
    table = np.zeros((tile_rows * tile_cols, (tile_rows + 2) * grid_cols), np.float32)
    for a in range(tile_rows):
        for b in range(tile_cols):
            for da in range(3):
                for db in range(3):
                    table[a * tile_cols + b, (a + da) * grid_cols + (b + db)] = 1.0
    return table


def exchange(value, extra, axis, xor, split_axis):
    count = lax.axis_size(axis)
    mine = (lax.axis_index(axis) // xor) % 2
    low = lax.index_in_dim(value, 0, split_axis, keepdims=False)
    high = lax.index_in_dim(value, 1, split_axis, keepdims=False)
    keep = jnp.where(mine == 1, high, low)
    send = jnp.where(mine == 1, low, high)
    pairs = [(i, i ^ xor) for i in range(count)]
    got, got_extra = lax.ppermute((send.astype(BF16), extra), axis, pairs)
    return keep + got.astype(F32), extra + got_extra


def reduce_weights(combined, extra):
    model_width = combined.shape[0]
    part = lax.psum_scatter(combined.astype(BF16), "dp", scatter_dimension=0, tiled=True).astype(F32)
    rows, cols = lax.axis_size("row"), lax.axis_size("col")
    rest = part.shape[0]
    value = part.reshape(rest, rows // 2, 2, cols // 2, 2, -1).transpose(1, 2, 3, 4, 0, 5)
    value, extra = exchange(value, extra, "row", 1, 1)
    value, extra = exchange(value, extra, "row", 2, 0)
    value, extra = exchange(value, extra, "col", 1, 1)
    value, extra = exchange(value, extra, "col", 2, 0)
    return value, extra


def local(latent, norm_shift, norm_scale, branch_gate, query_key_value, output_weight, tile_valid, cotangent):
    _, height, across, model_width = latent.shape
    tile_rows, tile_cols = height // TILE, across // TILE
    tiles = tile_rows * tile_cols
    tokens = tiles * CELLS
    heads = model_width // HEAD_DIM
    grid_tiles = (tile_rows + 2) * (tile_cols + 2)

    mask_whole = jnp.pad(tile_valid[0].astype(F32), ((1, 1), (1, 1)))
    row_start = lax.axis_index("row") * tile_rows
    col_start = lax.axis_index("col") * tile_cols
    mask_pad = lax.dynamic_slice(mask_whole, (row_start, col_start), (tile_rows + 2, tile_cols + 2))
    key_mask = jnp.asarray(neighbour_table(tile_rows, tile_cols)) * mask_pad.reshape(1, grid_tiles)
    token_key_mask = jnp.repeat(jnp.repeat(key_mask, CELLS, axis=0), CELLS, axis=1)
    query_valid = mask_pad[1:-1, 1:-1].reshape(tiles)
    token_valid = jnp.repeat(query_valid, CELLS)[:, None]

    image = to_tiles(latent[0])
    incoming = to_tiles(cotangent[0]).astype(F32)
    values = image.astype(F32)
    center = values - jnp.mean(values, axis=-1, keepdims=True)
    inverse = lax.rsqrt(jnp.mean(center * center, axis=-1, keepdims=True) + EPSILON)
    normed = center * inverse
    scale_one = 1.0 + norm_scale
    modulated = (normed * scale_one + norm_shift).astype(BF16)
    projections = jnp.dot(modulated, query_key_value, preferred_element_type=F32).astype(BF16)

    queries = projections[:, :model_width]
    key_value = projections[:, model_width:].reshape(tile_rows, tile_cols, CELLS, 2 * model_width)
    grid = halo(key_value).reshape(grid_tiles * CELLS, 2 * model_width)

    q_h = queries.reshape(tokens, heads, HEAD_DIM).transpose(1, 0, 2)
    k_h = grid[:, :model_width].reshape(-1, heads, HEAD_DIM).transpose(1, 0, 2)
    v_h = grid[:, model_width:].reshape(-1, heads, HEAD_DIM).transpose(1, 0, 2)

    scale = 1.0 / math.sqrt(HEAD_DIM)
    scores = jnp.einsum("hqe,hke->hqk", q_h, k_h, preferred_element_type=F32) * scale
    unnormed = jnp.where(token_key_mask[None] > 0.0, jnp.exp(scores), 0.0)
    denominator = jnp.sum(unnormed, axis=-1, keepdims=True) + (1.0 - token_valid)[None]
    attention = (unnormed / denominator).astype(BF16)
    attended_h = jnp.einsum("hqk,hke->hqe", attention, v_h, preferred_element_type=F32) * token_valid[None]
    attended = attended_h.astype(BF16).transpose(1, 0, 2).reshape(tokens, model_width)

    projected = jnp.dot(attended, output_weight, preferred_element_type=F32)
    gate_term = jnp.sum(incoming * projected, axis=0)
    grad_projected = (incoming * branch_gate).astype(BF16)
    output_term = jnp.einsum("nd,nf->df", attended, grad_projected, preferred_element_type=F32)
    grad_image = jnp.einsum("nf,df->nd", grad_projected, output_weight, preferred_element_type=F32)
    grad_attended = (grad_image * token_valid).astype(BF16)
    ga_h = grad_attended.reshape(tokens, heads, HEAD_DIM).transpose(1, 0, 2)

    grad_weights = jnp.einsum("hqe,hke->hqk", ga_h, v_h, preferred_element_type=F32)
    attention_wide = attention.astype(F32)
    row_inner = jnp.sum(attention_wide * grad_weights, axis=-1, keepdims=True)
    grad_scores = (attention_wide * (grad_weights - row_inner) * scale).astype(BF16)
    grad_q = jnp.einsum("hqk,hke->hqe", grad_scores, k_h, preferred_element_type=F32).astype(BF16)
    grad_k = jnp.einsum("hqk,hqe->hke", grad_scores, q_h, preferred_element_type=F32)
    grad_v = jnp.einsum("hqk,hqe->hke", attention, ga_h, preferred_element_type=F32)
    grad_k = grad_k.transpose(1, 0, 2).reshape(tile_rows + 2, tile_cols + 2, CELLS, model_width)
    grad_v = grad_v.transpose(1, 0, 2).reshape(tile_rows + 2, tile_cols + 2, CELLS, model_width)
    pair_grid = jnp.concatenate([grad_k, grad_v], axis=-1)
    pair_grads = return_rims(pair_grid).reshape(tokens, 2 * model_width)

    query_flat = grad_q.transpose(1, 0, 2).reshape(tokens, model_width)
    grad_all = jnp.concatenate([query_flat, pair_grads.astype(BF16)], axis=-1)
    input_term = jnp.einsum("nd,nf->df", modulated, grad_all, preferred_element_type=F32)
    grad_modulated = jnp.einsum("nf,df->nd", grad_all, query_key_value, preferred_element_type=F32)
    shift_term = jnp.sum(grad_modulated, axis=0)
    scale_term = jnp.sum(grad_modulated * normed, axis=0)
    grad_normed = grad_modulated * scale_one
    latent_term = inverse * (
        grad_normed
        - jnp.mean(grad_normed, axis=-1, keepdims=True)
        - normed * jnp.mean(grad_normed * normed, axis=-1, keepdims=True)
    )

    mixed = (values + branch_gate * projected).astype(BF16)
    latent_grad = (incoming + latent_term).astype(BF16)

    blocks = lax.axis_size("row") * lax.axis_size("col")
    width_in = input_term.shape[1] // blocks
    width_out = output_term.shape[1] // blocks
    combined = jnp.concatenate(
        [
            input_term.reshape(model_width, blocks, width_in),
            output_term.reshape(model_width, blocks, width_out),
        ],
        axis=-1,
    ).reshape(model_width, blocks * (width_in + width_out))
    reduced, sums = reduce_weights(combined, jnp.stack([shift_term, scale_term, gate_term]))
    input_grad = reduced[:, :width_in]
    output_grad = reduced[:, width_in:]

    return (
        from_tiles(mixed, height, across)[None],
        from_tiles(latent_grad, height, across)[None],
        input_grad,
        output_grad,
        sums[0:1],
        sums[1:2],
        sums[2:3],
    )


def solution(mesh):
    placed = (
        P("dp", "row", "col", None),
        P("dp", None),
        P("dp", None),
        P("dp", None),
        P(),
        P(),
        P("dp", None, None),
        P("dp", "row", "col", None),
    )
    return jax.shard_map(
        local,
        mesh=mesh,
        in_specs=placed,
        out_specs=(
            P("dp", "row", "col", None),
            P("dp", "row", "col", None),
            P("dp", ("row", "col")),
            P("dp", ("row", "col")),
            P("dp", None),
            P("dp", None),
            P("dp", None),
        ),
        check_vma=False,
    )
```

```python
import math

import jax
import jax.numpy as jnp
import numpy as np
from jax import lax
from jax.sharding import PartitionSpec as P
from jax.experimental import pallas as pl
from jax.experimental.pallas import tpu as pltpu

HEAD_DIM = 64
TILE = 8
CELLS = TILE * TILE
EPSILON = 1e-06
F32 = jnp.float32
BF16 = jnp.bfloat16


def to_tiles(image):
    rows, cols, features = image.shape
    blocks = image.reshape(rows // TILE, TILE, cols // TILE, TILE, features)
    blocks = blocks.transpose(0, 2, 1, 3, 4)
    return blocks.reshape((rows // TILE) * (cols // TILE) * CELLS, features)


def from_tiles(flat, rows, cols):
    features = flat.shape[-1]
    blocks = flat.reshape(rows // TILE, cols // TILE, TILE, TILE, features)
    blocks = blocks.transpose(0, 2, 1, 3, 4)
    return blocks.reshape(rows, cols, features)


def forward_pairs(count):
    return [(i, i + 1) for i in range(count - 1)]


def backward_pairs(count):
    return [(i + 1, i) for i in range(count - 1)]


def halo(grid):
    rows, cols = lax.axis_size("row"), lax.axis_size("col")
    from_above = lax.ppermute(grid[-1:], "row", forward_pairs(rows))
    from_below = lax.ppermute(grid[:1], "row", backward_pairs(rows))
    grid = jnp.concatenate([from_above, grid, from_below], axis=0)
    from_left = lax.ppermute(grid[:, -1:], "col", forward_pairs(cols))
    from_right = lax.ppermute(grid[:, :1], "col", backward_pairs(cols))
    return jnp.concatenate([from_left, grid, from_right], axis=1)


def return_rims(grid):
    rows, cols = lax.axis_size("row"), lax.axis_size("col")
    tile_rows, tile_cols = grid.shape[0] - 2, grid.shape[1] - 2
    from_right = lax.ppermute(grid[:, :1].astype(BF16), "col", backward_pairs(cols))
    from_left = lax.ppermute(grid[:, -1:].astype(BF16), "col", forward_pairs(cols))
    middle = grid[:, 1:-1]
    pad_c = ((0, 0), (0, tile_cols - 1), (0, 0), (0, 0))
    middle = middle + jnp.pad(from_left.astype(F32), pad_c)
    middle = middle + jnp.pad(from_right.astype(F32), (pad_c[0], pad_c[1][::-1], pad_c[2], pad_c[3]))
    from_below = lax.ppermute(middle[:1].astype(BF16), "row", backward_pairs(rows))
    from_above = lax.ppermute(middle[-1:].astype(BF16), "row", forward_pairs(rows))
    inner = middle[1:-1]
    pad_r = ((0, tile_rows - 1), (0, 0), (0, 0), (0, 0))
    inner = inner + jnp.pad(from_above.astype(F32), pad_r)
    inner = inner + jnp.pad(from_below.astype(F32), (pad_r[0][::-1], pad_r[1], pad_r[2], pad_r[3]))
    return inner


def neighbour_table(tile_rows, tile_cols):
    grid_cols = tile_cols + 2
    table = np.zeros((tile_rows * tile_cols, (tile_rows + 2) * grid_cols), np.float32)
    for a in range(tile_rows):
        for b in range(tile_cols):
            for da in range(3):
                for db in range(3):
                    table[a * tile_cols + b, (a + da) * grid_cols + (b + db)] = 1.0
    return table


def exchange(value, extra, axis, xor, split_axis):
    count = lax.axis_size(axis)
    mine = (lax.axis_index(axis) // xor) % 2
    low = lax.index_in_dim(value, 0, split_axis, keepdims=False)
    high = lax.index_in_dim(value, 1, split_axis, keepdims=False)
    keep = jnp.where(mine == 1, high, low)
    send = jnp.where(mine == 1, low, high)
    pairs = [(i, i ^ xor) for i in range(count)]
    got, got_extra = lax.ppermute((send.astype(BF16), extra), axis, pairs)
    return keep + got.astype(F32), extra + got_extra


def reduce_weights(combined, extra):
    model_width = combined.shape[0]
    part = lax.psum_scatter(combined.astype(BF16), "dp", scatter_dimension=0, tiled=True).astype(F32)
    rows, cols = lax.axis_size("row"), lax.axis_size("col")
    rest = part.shape[0]
    value = part.reshape(rest, rows // 2, 2, cols // 2, 2, -1).transpose(1, 2, 3, 4, 0, 5)
    value, extra = exchange(value, extra, "row", 1, 1)
    value, extra = exchange(value, extra, "row", 2, 0)
    value, extra = exchange(value, extra, "col", 1, 1)
    value, extra = exchange(value, extra, "col", 2, 0)
    return value, extra


def attention_kernel(q_ref, kv_ref, ga_ref, mask_ref, valid_ref, att_ref, gq_ref, gkv_ref):
    model_width = q_ref.shape[1]
    pair = 2 * HEAD_DIM
    scale = 1.0 / math.sqrt(HEAD_DIM)
    keep = mask_ref[...] > 0.0
    valid = valid_ref[...]
    empty = 1.0 - valid
    lane = lax.broadcasted_iota(jnp.int32, (1, pair), 1)
    first = lane < HEAD_DIM
    for p in range(model_width // pair):
        cols = slice(p * pair, (p + 1) * pair)
        q2 = q_ref[:, cols]
        k2 = kv_ref[:, cols]
        v2 = kv_ref[:, model_width + p * pair : model_width + (p + 1) * pair]
        ga2 = ga_ref[:, cols]
        outs = []
        for j in range(2):
            side = first if j == 0 else jnp.logical_not(first)
            qj = jnp.where(side, q2, jnp.zeros_like(q2))
            gaj = jnp.where(side, ga2, jnp.zeros_like(ga2))
            scores = lax.dot_general(qj, k2, (((1,), (1,)), ((), ())), preferred_element_type=F32) * scale
            unnormed = jnp.where(keep, jnp.exp(scores), 0.0)
            denominator = jnp.sum(unnormed, axis=1, keepdims=True) + empty
            attention = (unnormed / denominator).astype(BF16)
            attended = jnp.dot(attention, v2, preferred_element_type=F32)
            weights = lax.dot_general(gaj, v2, (((1,), (1,)), ((), ())), preferred_element_type=F32)
            wide = attention.astype(F32)
            inner = jnp.sum(wide * weights, axis=1, keepdims=True)
            grad_scores = (wide * (weights - inner) * scale).astype(BF16)
            gq = jnp.dot(grad_scores, k2, preferred_element_type=F32)
            gk = jnp.dot(grad_scores.T, qj, preferred_element_type=F32)
            gv = jnp.dot(attention.T, gaj, preferred_element_type=F32)
            outs.append((attended, gq, gk, gv))
        (a0, q0, k0, v0), (a1, q1, k1, v1) = outs
        att_ref[:, cols] = (jnp.where(first, a0, a1) * valid).astype(att_ref.dtype)
        gq_ref[:, cols] = jnp.where(first, q0, q1).astype(gq_ref.dtype)
        gkv_ref[:, cols] = jnp.where(first, k0, k1)
        gkv_ref[:, model_width + p * pair : model_width + (p + 1) * pair] = jnp.where(first, v0, v1)


def attention(queries, grid, grad_attended, token_key_mask, token_valid):
    tokens, model_width = queries.shape
    keys = grid.shape[0]
    whole = pl.BlockSpec(memory_space=pltpu.VMEM)
    flops = 2 * 2 * tokens * keys * 2 * model_width * 5
    return pl.pallas_call(
        attention_kernel,
        out_shape=(
            jax.ShapeDtypeStruct((tokens, model_width), BF16),
            jax.ShapeDtypeStruct((tokens, model_width), BF16),
            jax.ShapeDtypeStruct((keys, 2 * model_width), F32),
        ),
        in_specs=[whole] * 5,
        out_specs=(whole, whole, whole),
        compiler_params=pltpu.CompilerParams(vmem_limit_bytes=48 * 1024 * 1024),
        cost_estimate=pl.CostEstimate(flops=flops, transcendentals=2 * tokens * keys * model_width // HEAD_DIM, bytes_accessed=12 * 1024 * 1024),
    )(queries, grid, grad_attended, token_key_mask, token_valid)


def local(latent, norm_shift, norm_scale, branch_gate, query_key_value, output_weight, tile_valid, cotangent):
    _, height, across, model_width = latent.shape
    tile_rows, tile_cols = height // TILE, across // TILE
    tiles = tile_rows * tile_cols
    tokens = tiles * CELLS
    heads = model_width // HEAD_DIM
    grid_tiles = (tile_rows + 2) * (tile_cols + 2)

    mask_whole = jnp.pad(tile_valid[0].astype(F32), ((1, 1), (1, 1)))
    row_start = lax.axis_index("row") * tile_rows
    col_start = lax.axis_index("col") * tile_cols
    mask_pad = lax.dynamic_slice(mask_whole, (row_start, col_start), (tile_rows + 2, tile_cols + 2))
    key_mask = jnp.asarray(neighbour_table(tile_rows, tile_cols)) * mask_pad.reshape(1, grid_tiles)
    token_key_mask = jnp.repeat(jnp.repeat(key_mask, CELLS, axis=0), CELLS, axis=1)
    query_valid = mask_pad[1:-1, 1:-1].reshape(tiles)
    token_valid = jnp.repeat(query_valid, CELLS)[:, None]

    image = to_tiles(latent[0])
    incoming = to_tiles(cotangent[0]).astype(F32)
    values = image.astype(F32)
    center = values - jnp.mean(values, axis=-1, keepdims=True)
    inverse = lax.rsqrt(jnp.mean(center * center, axis=-1, keepdims=True) + EPSILON)
    normed = center * inverse
    scale_one = 1.0 + norm_scale
    modulated = (normed * scale_one + norm_shift).astype(BF16)
    projections = jnp.dot(modulated, query_key_value, preferred_element_type=F32).astype(BF16)

    queries = projections[:, :model_width]
    key_value = projections[:, model_width:].reshape(tile_rows, tile_cols, CELLS, 2 * model_width)
    grid = halo(key_value).reshape(grid_tiles * CELLS, 2 * model_width)

    grad_projected = (incoming * branch_gate).astype(BF16)
    grad_image = jnp.einsum("nf,df->nd", grad_projected, output_weight, preferred_element_type=F32)
    grad_attended = (grad_image * token_valid).astype(BF16)
    attended, grad_q, pair_grid = attention(queries, grid, grad_attended, token_key_mask, token_valid)

    projected = jnp.dot(attended, output_weight, preferred_element_type=F32)
    gate_term = jnp.sum(incoming * projected, axis=0)
    output_term = jnp.einsum("nd,nf->df", attended, grad_projected, preferred_element_type=F32)
    pair_grid = pair_grid.reshape(tile_rows + 2, tile_cols + 2, CELLS, 2 * model_width)
    pair_grads = return_rims(pair_grid).reshape(tokens, 2 * model_width)

    grad_all = jnp.concatenate([grad_q, pair_grads.astype(BF16)], axis=-1)
    input_term = jnp.einsum("nd,nf->df", modulated, grad_all, preferred_element_type=F32)
    grad_modulated = jnp.einsum("nf,df->nd", grad_all, query_key_value, preferred_element_type=F32)
    shift_term = jnp.sum(grad_modulated, axis=0)
    scale_term = jnp.sum(grad_modulated * normed, axis=0)
    grad_normed = grad_modulated * scale_one
    latent_term = inverse * (
        grad_normed
        - jnp.mean(grad_normed, axis=-1, keepdims=True)
        - normed * jnp.mean(grad_normed * normed, axis=-1, keepdims=True)
    )

    mixed = (values + branch_gate * projected).astype(BF16)
    latent_grad = (incoming + latent_term).astype(BF16)

    blocks = lax.axis_size("row") * lax.axis_size("col")
    width_in = input_term.shape[1] // blocks
    width_out = output_term.shape[1] // blocks
    combined = jnp.concatenate(
        [
            input_term.reshape(model_width, blocks, width_in),
            output_term.reshape(model_width, blocks, width_out),
        ],
        axis=-1,
    ).reshape(model_width, blocks * (width_in + width_out))
    reduced, sums = reduce_weights(combined, jnp.stack([shift_term, scale_term, gate_term]))
    input_grad = reduced[:, :width_in]
    output_grad = reduced[:, width_in:]

    return (
        from_tiles(mixed, height, across)[None],
        from_tiles(latent_grad, height, across)[None],
        input_grad,
        output_grad,
        sums[0:1],
        sums[1:2],
        sums[2:3],
    )


def solution(mesh):
    placed = (
        P("dp", "row", "col", None),
        P("dp", None),
        P("dp", None),
        P("dp", None),
        P(),
        P(),
        P("dp", None, None),
        P("dp", "row", "col", None),
    )
    return jax.shard_map(
        local,
        mesh=mesh,
        in_specs=placed,
        out_specs=(
            P("dp", "row", "col", None),
            P("dp", "row", "col", None),
            P("dp", ("row", "col")),
            P("dp", ("row", "col")),
            P("dp", None),
            P("dp", None),
            P("dp", None),
        ),
        check_vma=False,
    )
```

```python
import math

import jax
import jax.numpy as jnp
import numpy as np
from jax import lax
from jax.sharding import PartitionSpec as P
from jax.experimental import pallas as pl
from jax.experimental.pallas import tpu as pltpu

HEAD_DIM = 64
TILE = 8
CELLS = TILE * TILE
EPSILON = 1e-06
F32 = jnp.float32
BF16 = jnp.bfloat16


def to_tiles(image):
    rows, cols, features = image.shape
    blocks = image.reshape(rows // TILE, TILE, cols // TILE, TILE, features)
    blocks = blocks.transpose(0, 2, 1, 3, 4)
    return blocks.reshape((rows // TILE) * (cols // TILE) * CELLS, features)


def from_tiles(flat, rows, cols):
    features = flat.shape[-1]
    blocks = flat.reshape(rows // TILE, cols // TILE, TILE, TILE, features)
    blocks = blocks.transpose(0, 2, 1, 3, 4)
    return blocks.reshape(rows, cols, features)


def forward_pairs(count):
    return [(i, i + 1) for i in range(count - 1)]


def backward_pairs(count):
    return [(i + 1, i) for i in range(count - 1)]


def shifts(rows, cols, step_row, step_col):
    pairs = []
    for r in range(rows):
        for c in range(cols):
            r2, c2 = r + step_row, c + step_col
            if 0 <= r2 < rows and 0 <= c2 < cols:
                pairs.append((r * cols + c, r2 * cols + c2))
    return pairs


def send(block, step_row, step_col):
    rows, cols = lax.axis_size("row"), lax.axis_size("col")
    return lax.ppermute(block, ("row", "col"), shifts(rows, cols, step_row, step_col))


def halo(grid):
    top = send(grid[-1:], 1, 0)
    bottom = send(grid[:1], -1, 0)
    left = send(grid[:, -1:], 0, 1)
    right = send(grid[:, :1], 0, -1)
    top_left = send(grid[-1:, -1:], 1, 1)
    top_right = send(grid[-1:, :1], 1, -1)
    bottom_left = send(grid[:1, -1:], -1, 1)
    bottom_right = send(grid[:1, :1], -1, -1)
    upper = jnp.concatenate([top_left, top, top_right], axis=1)
    middle = jnp.concatenate([left, grid, right], axis=1)
    lower = jnp.concatenate([bottom_left, bottom, bottom_right], axis=1)
    return jnp.concatenate([upper, middle, lower], axis=0)


def place(block, tile_rows, tile_cols, at_row, at_col):
    def side(at, count):
        if at is None:
            return (0, 0)
        return (0, count - 1) if at == 0 else (count - 1, 0)

    rest = [(0, 0)] * (block.ndim - 2)
    return jnp.pad(block.astype(F32), [side(at_row, tile_rows), side(at_col, tile_cols)] + rest)


def return_rims(grid):
    tile_rows, tile_cols = grid.shape[0] - 2, grid.shape[1] - 2
    inner = grid[1:-1, 1:-1]
    parts = [
        (grid[:1, 1:-1], -1, 0, -1, None),
        (grid[-1:, 1:-1], 1, 0, 0, None),
        (grid[1:-1, :1], 0, -1, None, -1),
        (grid[1:-1, -1:], 0, 1, None, 0),
        (grid[:1, :1], -1, -1, -1, -1),
        (grid[:1, -1:], -1, 1, -1, 0),
        (grid[-1:, :1], 1, -1, 0, -1),
        (grid[-1:, -1:], 1, 1, 0, 0),
    ]
    received = [(send(block.astype(BF16), dr, dc), at_row, at_col) for block, dr, dc, at_row, at_col in parts]
    for block, at_row, at_col in received:
        inner = inner + place(block, tile_rows, tile_cols, at_row, at_col)
    return inner


def neighbour_table(tile_rows, tile_cols):
    grid_cols = tile_cols + 2
    table = np.zeros((tile_rows * tile_cols, (tile_rows + 2) * grid_cols), np.float32)
    for a in range(tile_rows):
        for b in range(tile_cols):
            for da in range(3):
                for db in range(3):
                    table[a * tile_cols + b, (a + da) * grid_cols + (b + db)] = 1.0
    return table


def exchange(value, extra, axis, xor, split_axis):
    count = lax.axis_size(axis)
    mine = (lax.axis_index(axis) // xor) % 2
    low = lax.index_in_dim(value, 0, split_axis, keepdims=False)
    high = lax.index_in_dim(value, 1, split_axis, keepdims=False)
    keep = jnp.where(mine == 1, high, low)
    away = jnp.where(mine == 1, low, high)
    pairs = [(i, i ^ xor) for i in range(count)]
    if extra is None:
        return keep + lax.ppermute(away.astype(BF16), axis, pairs).astype(F32), None
    got, got_extra = lax.ppermute((away.astype(BF16), extra), axis, pairs)
    return keep + got.astype(F32), extra + got_extra


def reduce_weights(term, extra):
    part = lax.psum_scatter(term.astype(BF16), "dp", scatter_dimension=0, tiled=True).astype(F32)
    rows, cols = lax.axis_size("row"), lax.axis_size("col")
    rest = part.shape[0]
    value = part.reshape(rest, rows // 2, 2, cols // 2, 2, -1).transpose(1, 2, 3, 4, 0, 5)
    value, extra = exchange(value, extra, "row", 1, 1)
    value, extra = exchange(value, extra, "row", 2, 0)
    value, extra = exchange(value, extra, "col", 1, 1)
    value, extra = exchange(value, extra, "col", 2, 0)
    return value, extra


def attention_kernel(q_ref, kv_ref, ga_ref, mask_ref, valid_ref, att_ref, gq_ref, gkv_ref):
    model_width = q_ref.shape[1]
    pair = 2 * HEAD_DIM
    scale = 1.0 / math.sqrt(HEAD_DIM)
    keep = mask_ref[...] > 0.0
    valid = valid_ref[...]
    empty = 1.0 - valid
    lane = lax.broadcasted_iota(jnp.int32, (1, pair), 1)
    first = lane < HEAD_DIM
    for p in range(model_width // pair):
        cols = slice(p * pair, (p + 1) * pair)
        q2 = q_ref[:, cols]
        k2 = kv_ref[:, cols]
        v2 = kv_ref[:, model_width + p * pair : model_width + (p + 1) * pair]
        ga2 = ga_ref[:, cols]
        outs = []
        for j in range(2):
            side = first if j == 0 else jnp.logical_not(first)
            qj = jnp.where(side, q2, jnp.zeros_like(q2))
            gaj = jnp.where(side, ga2, jnp.zeros_like(ga2))
            scores = lax.dot_general(qj, k2, (((1,), (1,)), ((), ())), preferred_element_type=F32) * scale
            unnormed = jnp.where(keep, jnp.exp(scores), 0.0)
            denominator = jnp.sum(unnormed, axis=1, keepdims=True) + empty
            attention = (unnormed / denominator).astype(BF16)
            attended = jnp.dot(attention, v2, preferred_element_type=F32)
            weights = lax.dot_general(gaj, v2, (((1,), (1,)), ((), ())), preferred_element_type=F32)
            wide = attention.astype(F32)
            inner = jnp.sum(wide * weights, axis=1, keepdims=True)
            grad_scores = (wide * (weights - inner) * scale).astype(BF16)
            gq = jnp.dot(grad_scores, k2, preferred_element_type=F32)
            gk = jnp.dot(grad_scores.T, qj, preferred_element_type=F32)
            gv = jnp.dot(attention.T, gaj, preferred_element_type=F32)
            outs.append((attended, gq, gk, gv))
        (a0, q0, k0, v0), (a1, q1, k1, v1) = outs
        att_ref[:, cols] = (jnp.where(first, a0, a1) * valid).astype(att_ref.dtype)
        gq_ref[:, cols] = jnp.where(first, q0, q1).astype(gq_ref.dtype)
        gkv_ref[:, cols] = jnp.where(first, k0, k1)
        gkv_ref[:, model_width + p * pair : model_width + (p + 1) * pair] = jnp.where(first, v0, v1)


def attention(queries, grid, grad_attended, token_key_mask, token_valid):
    tokens, model_width = queries.shape
    keys = grid.shape[0]
    whole = pl.BlockSpec(memory_space=pltpu.VMEM)
    flops = 2 * 2 * tokens * keys * 2 * model_width * 5
    return pl.pallas_call(
        attention_kernel,
        out_shape=(
            jax.ShapeDtypeStruct((tokens, model_width), BF16),
            jax.ShapeDtypeStruct((tokens, model_width), BF16),
            jax.ShapeDtypeStruct((keys, 2 * model_width), F32),
        ),
        in_specs=[whole] * 5,
        out_specs=(whole, whole, whole),
        compiler_params=pltpu.CompilerParams(vmem_limit_bytes=48 * 1024 * 1024),
        cost_estimate=pl.CostEstimate(flops=flops, transcendentals=2 * tokens * keys * model_width // HEAD_DIM, bytes_accessed=12 * 1024 * 1024),
    )(queries, grid, grad_attended, token_key_mask, token_valid)


def local(latent, norm_shift, norm_scale, branch_gate, query_key_value, output_weight, tile_valid, cotangent):
    _, height, across, model_width = latent.shape
    tile_rows, tile_cols = height // TILE, across // TILE
    tiles = tile_rows * tile_cols
    tokens = tiles * CELLS
    heads = model_width // HEAD_DIM
    grid_tiles = (tile_rows + 2) * (tile_cols + 2)

    mask_whole = jnp.pad(tile_valid[0].astype(F32), ((1, 1), (1, 1)))
    row_start = lax.axis_index("row") * tile_rows
    col_start = lax.axis_index("col") * tile_cols
    mask_pad = lax.dynamic_slice(mask_whole, (row_start, col_start), (tile_rows + 2, tile_cols + 2))
    key_mask = jnp.asarray(neighbour_table(tile_rows, tile_cols)) * mask_pad.reshape(1, grid_tiles)
    token_key_mask = jnp.repeat(jnp.repeat(key_mask, CELLS, axis=0), CELLS, axis=1)
    query_valid = mask_pad[1:-1, 1:-1].reshape(tiles)
    token_valid = jnp.repeat(query_valid, CELLS)[:, None]

    image = to_tiles(latent[0])
    incoming = to_tiles(cotangent[0]).astype(F32)
    values = image.astype(F32)
    center = values - jnp.mean(values, axis=-1, keepdims=True)
    inverse = lax.rsqrt(jnp.mean(center * center, axis=-1, keepdims=True) + EPSILON)
    normed = center * inverse
    scale_one = 1.0 + norm_scale
    modulated = (normed * scale_one + norm_shift).astype(BF16)
    projections = jnp.dot(modulated, query_key_value, preferred_element_type=F32).astype(BF16)

    queries = projections[:, :model_width]
    key_value = projections[:, model_width:].reshape(tile_rows, tile_cols, CELLS, 2 * model_width)
    grid = halo(key_value).reshape(grid_tiles * CELLS, 2 * model_width)

    grad_projected = (incoming * branch_gate).astype(BF16)
    grad_image = jnp.einsum("nf,df->nd", grad_projected, output_weight, preferred_element_type=F32)
    grad_attended = (grad_image * token_valid).astype(BF16)
    attended, grad_q, pair_grid = attention(queries, grid, grad_attended, token_key_mask, token_valid)

    projected = jnp.dot(attended, output_weight, preferred_element_type=F32)
    gate_term = jnp.sum(incoming * projected, axis=0)
    output_term = jnp.einsum("nd,nf->df", attended, grad_projected, preferred_element_type=F32)
    pair_grid = pair_grid.reshape(tile_rows + 2, tile_cols + 2, CELLS, 2 * model_width)
    pair_grads = return_rims(pair_grid).reshape(tokens, 2 * model_width)

    grad_all = jnp.concatenate([grad_q, pair_grads.astype(BF16)], axis=-1)
    input_term = jnp.einsum("nd,nf->df", modulated, grad_all, preferred_element_type=F32)
    grad_modulated = jnp.einsum("nf,df->nd", grad_all, query_key_value, preferred_element_type=F32)
    shift_term = jnp.sum(grad_modulated, axis=0)
    scale_term = jnp.sum(grad_modulated * normed, axis=0)
    grad_normed = grad_modulated * scale_one
    latent_term = inverse * (
        grad_normed
        - jnp.mean(grad_normed, axis=-1, keepdims=True)
        - normed * jnp.mean(grad_normed * normed, axis=-1, keepdims=True)
    )

    mixed = (values + branch_gate * projected).astype(BF16)
    latent_grad = (incoming + latent_term).astype(BF16)

    output_grad, _ = reduce_weights(output_term, None)
    input_grad, sums = reduce_weights(input_term, jnp.stack([shift_term, scale_term, gate_term]))

    return (
        from_tiles(mixed, height, across)[None],
        from_tiles(latent_grad, height, across)[None],
        input_grad,
        output_grad,
        sums[0:1],
        sums[1:2],
        sums[2:3],
    )


def solution(mesh):
    placed = (
        P("dp", "row", "col", None),
        P("dp", None),
        P("dp", None),
        P("dp", None),
        P(),
        P(),
        P("dp", None, None),
        P("dp", "row", "col", None),
    )
    return jax.shard_map(
        local,
        mesh=mesh,
        in_specs=placed,
        out_specs=(
            P("dp", "row", "col", None),
            P("dp", "row", "col", None),
            P("dp", ("row", "col")),
            P("dp", ("row", "col")),
            P("dp", None),
            P("dp", None),
            P("dp", None),
        ),
        check_vma=False,
    )
```

```python
import math

import jax
import jax.numpy as jnp
import numpy as np
from jax import lax
from jax.sharding import PartitionSpec as P
from jax.experimental import pallas as pl
from jax.experimental.pallas import tpu as pltpu

HEAD_DIM = 64
TILE = 8
CELLS = TILE * TILE
EPSILON = 1e-06
F32 = jnp.float32
BF16 = jnp.bfloat16


def to_tiles(image):
    rows, cols, features = image.shape
    blocks = image.reshape(rows // TILE, TILE, cols // TILE, TILE, features)
    blocks = blocks.transpose(0, 2, 1, 3, 4)
    return blocks.reshape((rows // TILE) * (cols // TILE) * CELLS, features)


def from_tiles(flat, rows, cols):
    features = flat.shape[-1]
    blocks = flat.reshape(rows // TILE, cols // TILE, TILE, TILE, features)
    blocks = blocks.transpose(0, 2, 1, 3, 4)
    return blocks.reshape(rows, cols, features)


def forward_pairs(count):
    return [(i, i + 1) for i in range(count - 1)]


def backward_pairs(count):
    return [(i + 1, i) for i in range(count - 1)]


def shifts(rows, cols, step_row, step_col):
    pairs = []
    for r in range(rows):
        for c in range(cols):
            r2, c2 = r + step_row, c + step_col
            if 0 <= r2 < rows and 0 <= c2 < cols:
                pairs.append((r * cols + c, r2 * cols + c2))
    return pairs


def send(block, step_row, step_col):
    rows, cols = lax.axis_size("row"), lax.axis_size("col")
    return lax.ppermute(block, ("row", "col"), shifts(rows, cols, step_row, step_col))


def halo(grid):
    top = send(grid[-1:], 1, 0)
    bottom = send(grid[:1], -1, 0)
    left = send(grid[:, -1:], 0, 1)
    right = send(grid[:, :1], 0, -1)
    top_left = send(grid[-1:, -1:], 1, 1)
    top_right = send(grid[-1:, :1], 1, -1)
    bottom_left = send(grid[:1, -1:], -1, 1)
    bottom_right = send(grid[:1, :1], -1, -1)
    upper = jnp.concatenate([top_left, top, top_right], axis=1)
    middle = jnp.concatenate([left, grid, right], axis=1)
    lower = jnp.concatenate([bottom_left, bottom, bottom_right], axis=1)
    return jnp.concatenate([upper, middle, lower], axis=0)


def place(block, tile_rows, tile_cols, at_row, at_col):
    def side(at, count):
        if at is None:
            return (0, 0)
        return (0, count - 1) if at == 0 else (count - 1, 0)

    rest = [(0, 0)] * (block.ndim - 2)
    return jnp.pad(block.astype(F32), [side(at_row, tile_rows), side(at_col, tile_cols)] + rest)


def return_rims(grid):
    tile_rows, tile_cols = grid.shape[0] - 2, grid.shape[1] - 2
    inner = grid[1:-1, 1:-1]
    parts = [
        (grid[:1, 1:-1], -1, 0, -1, None),
        (grid[-1:, 1:-1], 1, 0, 0, None),
        (grid[1:-1, :1], 0, -1, None, -1),
        (grid[1:-1, -1:], 0, 1, None, 0),
        (grid[:1, :1], -1, -1, -1, -1),
        (grid[:1, -1:], -1, 1, -1, 0),
        (grid[-1:, :1], 1, -1, 0, -1),
        (grid[-1:, -1:], 1, 1, 0, 0),
    ]
    received = [(send(block.astype(BF16), dr, dc), at_row, at_col) for block, dr, dc, at_row, at_col in parts]
    for block, at_row, at_col in received:
        inner = inner + place(block, tile_rows, tile_cols, at_row, at_col)
    return inner


def neighbour_table(tile_rows, tile_cols):
    grid_cols = tile_cols + 2
    table = np.zeros((tile_rows * tile_cols, (tile_rows + 2) * grid_cols), np.float32)
    for a in range(tile_rows):
        for b in range(tile_cols):
            for da in range(3):
                for db in range(3):
                    table[a * tile_cols + b, (a + da) * grid_cols + (b + db)] = 1.0
    return table


def exchange(value, extra, axis, xor, split_axis):
    count = lax.axis_size(axis)
    mine = (lax.axis_index(axis) // xor) % 2
    low = lax.index_in_dim(value, 0, split_axis, keepdims=False)
    high = lax.index_in_dim(value, 1, split_axis, keepdims=False)
    keep = jnp.where(mine == 1, high, low)
    away = jnp.where(mine == 1, low, high)
    pairs = [(i, i ^ xor) for i in range(count)]
    if extra is None:
        return keep + lax.ppermute(away.astype(BF16), axis, pairs).astype(F32), None
    got, got_extra = lax.ppermute((away.astype(BF16), extra), axis, pairs)
    return keep + got.astype(F32), extra + got_extra


def reduce_weights(term, extra):
    part = lax.psum_scatter(term.astype(BF16), "dp", scatter_dimension=0, tiled=True).astype(F32)
    rows, cols = lax.axis_size("row"), lax.axis_size("col")
    rest = part.shape[0]
    value = part.reshape(rest, rows // 2, 2, cols // 2, 2, -1).transpose(1, 2, 3, 4, 0, 5)
    value, extra = exchange(value, extra, "row", 1, 1)
    value, extra = exchange(value, extra, "row", 2, 0)
    value, extra = exchange(value, extra, "col", 1, 1)
    value, extra = exchange(value, extra, "col", 2, 0)
    return value, extra


def attention_kernel(q_ref, kv_ref, ga_ref, mask_ref, valid_ref, att_ref, gq_ref, gkv_ref):
    model_width = q_ref.shape[1]
    pair = 2 * HEAD_DIM
    scale = 1.0 / math.sqrt(HEAD_DIM)
    keep = mask_ref[...] > 0.0
    valid = valid_ref[...]
    empty = 1.0 - valid
    lane = lax.broadcasted_iota(jnp.int32, (1, pair), 1)
    first = lane < HEAD_DIM
    for p in range(model_width // pair):
        cols = slice(p * pair, (p + 1) * pair)
        q2 = q_ref[:, cols]
        k2 = kv_ref[:, cols]
        v2 = kv_ref[:, model_width + p * pair : model_width + (p + 1) * pair]
        ga2 = ga_ref[:, cols]
        outs = []
        for j in range(2):
            side = first if j == 0 else jnp.logical_not(first)
            qj = jnp.where(side, q2, jnp.zeros_like(q2))
            gaj = jnp.where(side, ga2, jnp.zeros_like(ga2))
            scores = lax.dot_general(qj, k2, (((1,), (1,)), ((), ())), preferred_element_type=F32) * scale
            unnormed = jnp.where(keep, jnp.exp(scores), 0.0)
            denominator = jnp.sum(unnormed, axis=1, keepdims=True) + empty
            attention = (unnormed / denominator).astype(BF16)
            attended = jnp.dot(attention, v2, preferred_element_type=F32)
            weights = lax.dot_general(gaj, v2, (((1,), (1,)), ((), ())), preferred_element_type=F32)
            wide = attention.astype(F32)
            inner = jnp.sum(wide * weights, axis=1, keepdims=True)
            grad_scores = (wide * (weights - inner) * scale).astype(BF16)
            gq = jnp.dot(grad_scores, k2, preferred_element_type=F32)
            gk = jnp.dot(grad_scores.T, qj, preferred_element_type=F32)
            gv = jnp.dot(attention.T, gaj, preferred_element_type=F32)
            outs.append((attended, gq, gk, gv))
        (a0, q0, k0, v0), (a1, q1, k1, v1) = outs
        att_ref[:, cols] = (jnp.where(first, a0, a1) * valid).astype(att_ref.dtype)
        gq_ref[:, cols] = jnp.where(first, q0, q1).astype(gq_ref.dtype)
        gkv_ref[:, cols] = jnp.where(first, k0, k1)
        gkv_ref[:, model_width + p * pair : model_width + (p + 1) * pair] = jnp.where(first, v0, v1)


def attention(queries, grid, grad_attended, token_key_mask, token_valid):
    tokens, model_width = queries.shape
    keys = grid.shape[0]
    whole = pl.BlockSpec(memory_space=pltpu.VMEM)
    flops = 2 * 2 * tokens * keys * 2 * model_width * 5
    return pl.pallas_call(
        attention_kernel,
        out_shape=(
            jax.ShapeDtypeStruct((tokens, model_width), BF16),
            jax.ShapeDtypeStruct((tokens, model_width), BF16),
            jax.ShapeDtypeStruct((keys, 2 * model_width), F32),
        ),
        in_specs=[whole] * 5,
        out_specs=(whole, whole, whole),
        compiler_params=pltpu.CompilerParams(vmem_limit_bytes=48 * 1024 * 1024),
        cost_estimate=pl.CostEstimate(flops=flops, transcendentals=2 * tokens * keys * model_width // HEAD_DIM, bytes_accessed=12 * 1024 * 1024),
    )(queries, grid, grad_attended, token_key_mask, token_valid)


def local(latent, norm_shift, norm_scale, branch_gate, query_key_value, output_weight, tile_valid, cotangent):
    _, height, across, model_width = latent.shape
    tile_rows, tile_cols = height // TILE, across // TILE
    tiles = tile_rows * tile_cols
    tokens = tiles * CELLS
    heads = model_width // HEAD_DIM
    grid_tiles = (tile_rows + 2) * (tile_cols + 2)

    mask_whole = jnp.pad(tile_valid[0].astype(F32), ((1, 1), (1, 1)))
    row_start = lax.axis_index("row") * tile_rows
    col_start = lax.axis_index("col") * tile_cols
    mask_pad = lax.dynamic_slice(mask_whole, (row_start, col_start), (tile_rows + 2, tile_cols + 2))
    key_mask = jnp.asarray(neighbour_table(tile_rows, tile_cols)) * mask_pad.reshape(1, grid_tiles)
    token_key_mask = jnp.repeat(jnp.repeat(key_mask, CELLS, axis=0), CELLS, axis=1)
    query_valid = mask_pad[1:-1, 1:-1].reshape(tiles)
    token_valid = jnp.repeat(query_valid, CELLS)[:, None]

    image = to_tiles(latent[0])
    incoming = to_tiles(cotangent[0]).astype(F32)
    values = image.astype(F32)
    center = values - jnp.mean(values, axis=-1, keepdims=True)
    inverse = lax.rsqrt(jnp.mean(center * center, axis=-1, keepdims=True) + EPSILON)
    normed = center * inverse
    scale_one = 1.0 + norm_scale
    modulated = (normed * scale_one + norm_shift).astype(BF16)
    projections = jnp.dot(modulated, query_key_value, preferred_element_type=F32).astype(BF16)

    queries = projections[:, :model_width]
    key_value = projections[:, model_width:].reshape(tile_rows, tile_cols, CELLS, 2 * model_width)
    grid = halo(key_value).reshape(grid_tiles * CELLS, 2 * model_width)

    grad_projected = (incoming * branch_gate).astype(BF16)
    grad_image = jnp.einsum("nf,df->nd", grad_projected, output_weight, preferred_element_type=F32)
    grad_attended = (grad_image * token_valid).astype(BF16)
    attended, grad_q, pair_grid = attention(queries, grid, grad_attended, token_key_mask, token_valid)

    projected = jnp.dot(attended, output_weight, preferred_element_type=F32)
    gate_term = jnp.sum(incoming * projected, axis=0)
    output_term = jnp.einsum("nd,nf->df", attended, grad_projected, preferred_element_type=F32)
    pair_grid = pair_grid.reshape(tile_rows + 2, tile_cols + 2, CELLS, 2 * model_width)
    pair_grads = return_rims(pair_grid).reshape(tokens, 2 * model_width)

    grad_all = jnp.concatenate([grad_q, pair_grads.astype(BF16)], axis=-1)
    input_term = jnp.einsum("nd,nf->df", modulated, grad_all, preferred_element_type=F32)
    grad_modulated = jnp.einsum("nf,df->nd", grad_all, query_key_value, preferred_element_type=F32)
    shift_term = jnp.sum(grad_modulated, axis=0)
    scale_term = jnp.sum(grad_modulated * normed, axis=0)
    grad_normed = grad_modulated * scale_one
    latent_term = inverse * (
        grad_normed
        - jnp.mean(grad_normed, axis=-1, keepdims=True)
        - normed * jnp.mean(grad_normed * normed, axis=-1, keepdims=True)
    )

    mixed = (values + branch_gate * projected).astype(BF16)
    latent_grad = (incoming + latent_term).astype(BF16)

    blocks = lax.axis_size("row") * lax.axis_size("col")
    width_in = input_term.shape[1] // blocks
    width_out = output_term.shape[1] // blocks
    combined = jnp.concatenate(
        [
            input_term.reshape(model_width, blocks, width_in),
            output_term.reshape(model_width, blocks, width_out),
        ],
        axis=-1,
    ).reshape(model_width, blocks * (width_in + width_out))
    reduced, sums = reduce_weights(combined, jnp.stack([shift_term, scale_term, gate_term]))
    input_grad = reduced[:, :width_in]
    output_grad = reduced[:, width_in:]

    return (
        from_tiles(mixed, height, across)[None],
        from_tiles(latent_grad, height, across)[None],
        input_grad,
        output_grad,
        sums[0:1],
        sums[1:2],
        sums[2:3],
    )


def solution(mesh):
    placed = (
        P("dp", "row", "col", None),
        P("dp", None),
        P("dp", None),
        P("dp", None),
        P(),
        P(),
        P("dp", None, None),
        P("dp", "row", "col", None),
    )
    return jax.shard_map(
        local,
        mesh=mesh,
        in_specs=placed,
        out_specs=(
            P("dp", "row", "col", None),
            P("dp", "row", "col", None),
            P("dp", ("row", "col")),
            P("dp", ("row", "col")),
            P("dp", None),
            P("dp", None),
            P("dp", None),
        ),
        check_vma=False,
    )
```

```python
import math

import jax
import jax.numpy as jnp
import numpy as np
from jax import lax
from jax.sharding import PartitionSpec as P
from jax.experimental import pallas as pl
from jax.experimental.pallas import tpu as pltpu

HEAD_DIM = 64
TILE = 8
CELLS = TILE * TILE
EPSILON = 1e-06
F32 = jnp.float32
BF16 = jnp.bfloat16


def to_tiles(image):
    rows, cols, features = image.shape
    blocks = image.reshape(rows // TILE, TILE, cols // TILE, TILE, features)
    blocks = blocks.transpose(0, 2, 1, 3, 4)
    return blocks.reshape((rows // TILE) * (cols // TILE) * CELLS, features)


def from_tiles(flat, rows, cols):
    features = flat.shape[-1]
    blocks = flat.reshape(rows // TILE, cols // TILE, TILE, TILE, features)
    blocks = blocks.transpose(0, 2, 1, 3, 4)
    return blocks.reshape(rows, cols, features)


def forward_pairs(count):
    return [(i, i + 1) for i in range(count - 1)]


def backward_pairs(count):
    return [(i + 1, i) for i in range(count - 1)]


def shifts(rows, cols, step_row, step_col):
    pairs = []
    for r in range(rows):
        for c in range(cols):
            r2, c2 = r + step_row, c + step_col
            if 0 <= r2 < rows and 0 <= c2 < cols:
                pairs.append((r * cols + c, r2 * cols + c2))
    return pairs


def send(block, step_row, step_col):
    rows, cols = lax.axis_size("row"), lax.axis_size("col")
    return lax.ppermute(block, ("row", "col"), shifts(rows, cols, step_row, step_col))


def halo(grid):
    top = send(grid[-1:], 1, 0)
    bottom = send(grid[:1], -1, 0)
    left = send(grid[:, -1:], 0, 1)
    right = send(grid[:, :1], 0, -1)
    top_left = send(grid[-1:, -1:], 1, 1)
    top_right = send(grid[-1:, :1], 1, -1)
    bottom_left = send(grid[:1, -1:], -1, 1)
    bottom_right = send(grid[:1, :1], -1, -1)
    upper = jnp.concatenate([top_left, top, top_right], axis=1)
    middle = jnp.concatenate([left, grid, right], axis=1)
    lower = jnp.concatenate([bottom_left, bottom, bottom_right], axis=1)
    return jnp.concatenate([upper, middle, lower], axis=0)


def place(block, tile_rows, tile_cols, at_row, at_col):
    def side(at, count):
        if at is None:
            return (0, 0)
        return (0, count - 1) if at == 0 else (count - 1, 0)

    rest = [(0, 0)] * (block.ndim - 2)
    return jnp.pad(block.astype(F32), [side(at_row, tile_rows), side(at_col, tile_cols)] + rest)


def return_rims(grid):
    tile_rows, tile_cols = grid.shape[0] - 2, grid.shape[1] - 2
    inner = grid[1:-1, 1:-1]
    parts = [
        (grid[:1, 1:-1], -1, 0, -1, None),
        (grid[-1:, 1:-1], 1, 0, 0, None),
        (grid[1:-1, :1], 0, -1, None, -1),
        (grid[1:-1, -1:], 0, 1, None, 0),
        (grid[:1, :1], -1, -1, -1, -1),
        (grid[:1, -1:], -1, 1, -1, 0),
        (grid[-1:, :1], 1, -1, 0, -1),
        (grid[-1:, -1:], 1, 1, 0, 0),
    ]
    received = [(send(block.astype(BF16), dr, dc), at_row, at_col) for block, dr, dc, at_row, at_col in parts]
    for block, at_row, at_col in received:
        inner = inner + place(block, tile_rows, tile_cols, at_row, at_col)
    return inner


def neighbour_table(tile_rows, tile_cols):
    grid_cols = tile_cols + 2
    table = np.zeros((tile_rows * tile_cols, (tile_rows + 2) * grid_cols), np.float32)
    for a in range(tile_rows):
        for b in range(tile_cols):
            for da in range(3):
                for db in range(3):
                    table[a * tile_cols + b, (a + da) * grid_cols + (b + db)] = 1.0
    return table


def exchange(value, extra, axis, xor, split_axis):
    count = lax.axis_size(axis)
    mine = (lax.axis_index(axis) // xor) % 2
    low = lax.index_in_dim(value, 0, split_axis, keepdims=False)
    high = lax.index_in_dim(value, 1, split_axis, keepdims=False)
    keep = jnp.where(mine == 1, high, low)
    away = jnp.where(mine == 1, low, high)
    pairs = [(i, i ^ xor) for i in range(count)]
    if extra is None:
        return keep + lax.ppermute(away.astype(BF16), axis, pairs).astype(F32), None
    got, got_extra = lax.ppermute((away.astype(BF16), extra), axis, pairs)
    return keep + got.astype(F32), extra + got_extra


def scatter_dp(term):
    count = lax.axis_size("dp")
    bits = count.bit_length() - 1
    value = term.reshape((2,) * bits + (term.shape[0] // count,) + term.shape[1:])
    for step in range(bits):
        value, _ = exchange(value, None, "dp", 1 << step, bits - 1 - step)
    return value


def reduce_weights(term, extra, on_permutes=False):
    if on_permutes:
        part = scatter_dp(term)
    else:
        part = lax.psum_scatter(term.astype(BF16), "dp", scatter_dimension=0, tiled=True).astype(F32)
    rows, cols = lax.axis_size("row"), lax.axis_size("col")
    rest = part.shape[0]
    value = part.reshape(rest, rows // 2, 2, cols // 2, 2, -1).transpose(1, 2, 3, 4, 0, 5)
    value, extra = exchange(value, extra, "row", 1, 1)
    value, extra = exchange(value, extra, "row", 2, 0)
    value, extra = exchange(value, extra, "col", 1, 1)
    value, extra = exchange(value, extra, "col", 2, 0)
    return value, extra


def attention_kernel(q_ref, kv_ref, ga_ref, mask_ref, valid_ref, att_ref, gq_ref, gkv_ref):
    model_width = q_ref.shape[1]
    pair = 2 * HEAD_DIM
    scale = 1.0 / math.sqrt(HEAD_DIM)
    keep = mask_ref[...] > 0.0
    valid = valid_ref[...]
    empty = 1.0 - valid
    lane = lax.broadcasted_iota(jnp.int32, (1, pair), 1)
    first = lane < HEAD_DIM
    for p in range(model_width // pair):
        cols = slice(p * pair, (p + 1) * pair)
        q2 = q_ref[:, cols]
        k2 = kv_ref[:, cols]
        v2 = kv_ref[:, model_width + p * pair : model_width + (p + 1) * pair]
        ga2 = ga_ref[:, cols]
        outs = []
        for j in range(2):
            side = first if j == 0 else jnp.logical_not(first)
            qj = jnp.where(side, q2, jnp.zeros_like(q2))
            gaj = jnp.where(side, ga2, jnp.zeros_like(ga2))
            scores = lax.dot_general(qj, k2, (((1,), (1,)), ((), ())), preferred_element_type=F32) * scale
            unnormed = jnp.where(keep, jnp.exp(scores), 0.0)
            denominator = jnp.sum(unnormed, axis=1, keepdims=True) + empty
            attention = (unnormed / denominator).astype(BF16)
            attended = jnp.dot(attention, v2, preferred_element_type=F32)
            weights = lax.dot_general(gaj, v2, (((1,), (1,)), ((), ())), preferred_element_type=F32)
            wide = attention.astype(F32)
            inner = jnp.sum(wide * weights, axis=1, keepdims=True)
            grad_scores = (wide * (weights - inner) * scale).astype(BF16)
            gq = jnp.dot(grad_scores, k2, preferred_element_type=F32)
            gk = jnp.dot(grad_scores.T, qj, preferred_element_type=F32)
            gv = jnp.dot(attention.T, gaj, preferred_element_type=F32)
            outs.append((attended, gq, gk, gv))
        (a0, q0, k0, v0), (a1, q1, k1, v1) = outs
        att_ref[:, cols] = (jnp.where(first, a0, a1) * valid).astype(att_ref.dtype)
        gq_ref[:, cols] = jnp.where(first, q0, q1).astype(gq_ref.dtype)
        gkv_ref[:, cols] = jnp.where(first, k0, k1)
        gkv_ref[:, model_width + p * pair : model_width + (p + 1) * pair] = jnp.where(first, v0, v1)


def attention(queries, grid, grad_attended, token_key_mask, token_valid):
    tokens, model_width = queries.shape
    keys = grid.shape[0]
    whole = pl.BlockSpec(memory_space=pltpu.VMEM)
    flops = 2 * 2 * tokens * keys * 2 * model_width * 5
    return pl.pallas_call(
        attention_kernel,
        out_shape=(
            jax.ShapeDtypeStruct((tokens, model_width), BF16),
            jax.ShapeDtypeStruct((tokens, model_width), BF16),
            jax.ShapeDtypeStruct((keys, 2 * model_width), F32),
        ),
        in_specs=[whole] * 5,
        out_specs=(whole, whole, whole),
        compiler_params=pltpu.CompilerParams(vmem_limit_bytes=48 * 1024 * 1024),
        cost_estimate=pl.CostEstimate(flops=flops, transcendentals=2 * tokens * keys * model_width // HEAD_DIM, bytes_accessed=12 * 1024 * 1024),
    )(queries, grid, grad_attended, token_key_mask, token_valid)


def local(latent, norm_shift, norm_scale, branch_gate, query_key_value, output_weight, tile_valid, cotangent):
    _, height, across, model_width = latent.shape
    tile_rows, tile_cols = height // TILE, across // TILE
    tiles = tile_rows * tile_cols
    tokens = tiles * CELLS
    heads = model_width // HEAD_DIM
    grid_tiles = (tile_rows + 2) * (tile_cols + 2)

    mask_whole = jnp.pad(tile_valid[0].astype(F32), ((1, 1), (1, 1)))
    row_start = lax.axis_index("row") * tile_rows
    col_start = lax.axis_index("col") * tile_cols
    mask_pad = lax.dynamic_slice(mask_whole, (row_start, col_start), (tile_rows + 2, tile_cols + 2))
    key_mask = jnp.asarray(neighbour_table(tile_rows, tile_cols)) * mask_pad.reshape(1, grid_tiles)
    token_key_mask = jnp.repeat(jnp.repeat(key_mask, CELLS, axis=0), CELLS, axis=1)
    query_valid = mask_pad[1:-1, 1:-1].reshape(tiles)
    token_valid = jnp.repeat(query_valid, CELLS)[:, None]

    image = to_tiles(latent[0])
    incoming = to_tiles(cotangent[0]).astype(F32)
    values = image.astype(F32)
    center = values - jnp.mean(values, axis=-1, keepdims=True)
    inverse = lax.rsqrt(jnp.mean(center * center, axis=-1, keepdims=True) + EPSILON)
    normed = center * inverse
    scale_one = 1.0 + norm_scale
    modulated = (normed * scale_one + norm_shift).astype(BF16)
    projections = jnp.dot(modulated, query_key_value, preferred_element_type=F32).astype(BF16)

    queries = projections[:, :model_width]
    key_value = projections[:, model_width:].reshape(tile_rows, tile_cols, CELLS, 2 * model_width)
    grid = halo(key_value).reshape(grid_tiles * CELLS, 2 * model_width)

    grad_projected = (incoming * branch_gate).astype(BF16)
    grad_image = jnp.einsum("nf,df->nd", grad_projected, output_weight, preferred_element_type=F32)
    grad_attended = (grad_image * token_valid).astype(BF16)
    attended, grad_q, pair_grid = attention(queries, grid, grad_attended, token_key_mask, token_valid)

    projected = jnp.dot(attended, output_weight, preferred_element_type=F32)
    gate_term = jnp.sum(incoming * projected, axis=0)
    output_term = jnp.einsum("nd,nf->df", attended, grad_projected, preferred_element_type=F32)
    pair_grid = pair_grid.reshape(tile_rows + 2, tile_cols + 2, CELLS, 2 * model_width)
    pair_grads = return_rims(pair_grid).reshape(tokens, 2 * model_width)

    grad_all = jnp.concatenate([grad_q, pair_grads.astype(BF16)], axis=-1)
    input_term = jnp.einsum("nd,nf->df", modulated, grad_all, preferred_element_type=F32)
    grad_modulated = jnp.einsum("nf,df->nd", grad_all, query_key_value, preferred_element_type=F32)
    shift_term = jnp.sum(grad_modulated, axis=0)
    scale_term = jnp.sum(grad_modulated * normed, axis=0)
    grad_normed = grad_modulated * scale_one
    latent_term = inverse * (
        grad_normed
        - jnp.mean(grad_normed, axis=-1, keepdims=True)
        - normed * jnp.mean(grad_normed * normed, axis=-1, keepdims=True)
    )

    mixed = (values + branch_gate * projected).astype(BF16)
    latent_grad = (incoming + latent_term).astype(BF16)

    output_grad, _ = reduce_weights(output_term, None, on_permutes=True)
    input_grad, sums = reduce_weights(input_term, jnp.stack([shift_term, scale_term, gate_term]))

    return (
        from_tiles(mixed, height, across)[None],
        from_tiles(latent_grad, height, across)[None],
        input_grad,
        output_grad,
        sums[0:1],
        sums[1:2],
        sums[2:3],
    )


def solution(mesh):
    placed = (
        P("dp", "row", "col", None),
        P("dp", None),
        P("dp", None),
        P("dp", None),
        P(),
        P(),
        P("dp", None, None),
        P("dp", "row", "col", None),
    )
    return jax.shard_map(
        local,
        mesh=mesh,
        in_specs=placed,
        out_specs=(
            P("dp", "row", "col", None),
            P("dp", "row", "col", None),
            P("dp", ("row", "col")),
            P("dp", ("row", "col")),
            P("dp", None),
            P("dp", None),
            P("dp", None),
        ),
        check_vma=False,
    )
```

```python
import math

import jax
import jax.numpy as jnp
import numpy as np
from jax import lax
from jax.sharding import PartitionSpec as P
from jax.experimental import pallas as pl
from jax.experimental.pallas import tpu as pltpu

HEAD_DIM = 64
TILE = 8
CELLS = TILE * TILE
EPSILON = 1e-06
F32 = jnp.float32
BF16 = jnp.bfloat16


def to_tiles(image):
    rows, cols, features = image.shape
    blocks = image.reshape(rows // TILE, TILE, cols // TILE, TILE, features)
    blocks = blocks.transpose(0, 2, 1, 3, 4)
    return blocks.reshape((rows // TILE) * (cols // TILE) * CELLS, features)


def from_tiles(flat, rows, cols):
    features = flat.shape[-1]
    blocks = flat.reshape(rows // TILE, cols // TILE, TILE, TILE, features)
    blocks = blocks.transpose(0, 2, 1, 3, 4)
    return blocks.reshape(rows, cols, features)


def forward_pairs(count):
    return [(i, i + 1) for i in range(count - 1)]


def backward_pairs(count):
    return [(i + 1, i) for i in range(count - 1)]


def shifts(rows, cols, step_row, step_col):
    pairs = []
    for r in range(rows):
        for c in range(cols):
            r2, c2 = r + step_row, c + step_col
            if 0 <= r2 < rows and 0 <= c2 < cols:
                pairs.append((r * cols + c, r2 * cols + c2))
    return pairs


def send(block, step_row, step_col):
    rows, cols = lax.axis_size("row"), lax.axis_size("col")
    return lax.ppermute(block, ("row", "col"), shifts(rows, cols, step_row, step_col))


def halo(grid):
    top = send(grid[-1:], 1, 0)
    bottom = send(grid[:1], -1, 0)
    left = send(grid[:, -1:], 0, 1)
    right = send(grid[:, :1], 0, -1)
    top_left = send(grid[-1:, -1:], 1, 1)
    top_right = send(grid[-1:, :1], 1, -1)
    bottom_left = send(grid[:1, -1:], -1, 1)
    bottom_right = send(grid[:1, :1], -1, -1)
    upper = jnp.concatenate([top_left, top, top_right], axis=1)
    middle = jnp.concatenate([left, grid, right], axis=1)
    lower = jnp.concatenate([bottom_left, bottom, bottom_right], axis=1)
    return jnp.concatenate([upper, middle, lower], axis=0)


def place(block, tile_rows, tile_cols, at_row, at_col):
    def side(at, count):
        if at is None:
            return (0, 0)
        return (0, count - 1) if at == 0 else (count - 1, 0)

    rest = [(0, 0)] * (block.ndim - 2)
    return jnp.pad(block.astype(F32), [side(at_row, tile_rows), side(at_col, tile_cols)] + rest)


def return_rims(grid):
    tile_rows, tile_cols = grid.shape[0] - 2, grid.shape[1] - 2
    inner = grid[1:-1, 1:-1]
    parts = [
        (grid[:1, 1:-1], -1, 0, -1, None),
        (grid[-1:, 1:-1], 1, 0, 0, None),
        (grid[1:-1, :1], 0, -1, None, -1),
        (grid[1:-1, -1:], 0, 1, None, 0),
        (grid[:1, :1], -1, -1, -1, -1),
        (grid[:1, -1:], -1, 1, -1, 0),
        (grid[-1:, :1], 1, -1, 0, -1),
        (grid[-1:, -1:], 1, 1, 0, 0),
    ]
    received = [(send(block.astype(BF16), dr, dc), at_row, at_col) for block, dr, dc, at_row, at_col in parts]
    for block, at_row, at_col in received:
        inner = inner + place(block, tile_rows, tile_cols, at_row, at_col)
    return inner


def neighbour_table(tile_rows, tile_cols):
    grid_cols = tile_cols + 2
    table = np.zeros((tile_rows * tile_cols, (tile_rows + 2) * grid_cols), np.float32)
    for a in range(tile_rows):
        for b in range(tile_cols):
            for da in range(3):
                for db in range(3):
                    table[a * tile_cols + b, (a + da) * grid_cols + (b + db)] = 1.0
    return table


def exchange(value, extra, axis, xor, split_axis):
    count = lax.axis_size(axis)
    mine = (lax.axis_index(axis) // xor) % 2
    low = lax.index_in_dim(value, 0, split_axis, keepdims=False)
    high = lax.index_in_dim(value, 1, split_axis, keepdims=False)
    keep = jnp.where(mine == 1, high, low)
    away = jnp.where(mine == 1, low, high)
    pairs = [(i, i ^ xor) for i in range(count)]
    if extra is None:
        return keep + lax.ppermute(away.astype(BF16), axis, pairs).astype(F32), None
    got, got_extra = lax.ppermute((away.astype(BF16), extra), axis, pairs)
    return keep + got.astype(F32), extra + got_extra


def scatter_dp(term):
    count = lax.axis_size("dp")
    bits = count.bit_length() - 1
    value = term.reshape((2,) * bits + (term.shape[0] // count,) + term.shape[1:])
    for step in range(bits):
        value, _ = exchange(value, None, "dp", 1 << step, bits - 1 - step)
    return value


def reduce_weights(term, extra, on_permutes=False):
    if on_permutes:
        part = scatter_dp(term)
    else:
        part = lax.psum_scatter(term.astype(BF16), "dp", scatter_dimension=0, tiled=True).astype(F32)
    rows, cols = lax.axis_size("row"), lax.axis_size("col")
    rest = part.shape[0]
    value = part.reshape(rest, rows, cols, -1).transpose(1, 2, 0, 3)
    value, extra = exchange_all(value, extra, "row")
    value, extra = exchange_all(value, extra, "col")
    return value, extra


def exchange_all(value, extra, axis):
    count = lax.axis_size(axis)
    me = lax.axis_index(axis)
    total = lax.dynamic_index_in_dim(value, me, 0, keepdims=False)
    pieces = [(me, extra)]
    for shift in range(1, count):
        pairs = [(i, (i + shift) % count) for i in range(count)]
        block = lax.dynamic_index_in_dim(value, (me + shift) % count, 0, keepdims=False)
        if extra is None:
            got = lax.ppermute(block.astype(BF16), axis, pairs)
        else:
            got, got_extra = lax.ppermute((block.astype(BF16), extra), axis, pairs)
            pieces.append(((me - shift) % count, got_extra))
        total = total + got.astype(F32)
    if extra is None:
        return total, None
    summed = None
    for source in range(count):
        term = jnp.zeros_like(extra)
        for origin, piece in pieces:
            term = jnp.where(origin == source, piece, term)
        summed = term if summed is None else summed + term
    return total, summed


def attention_kernel(q_ref, kv_ref, ga_ref, mask_ref, valid_ref, att_ref, gq_ref, gkv_ref):
    model_width = q_ref.shape[1]
    pair = 2 * HEAD_DIM
    scale = 1.0 / math.sqrt(HEAD_DIM)
    keep = mask_ref[...] > 0.0
    valid = valid_ref[...]
    empty = 1.0 - valid
    lane = lax.broadcasted_iota(jnp.int32, (1, pair), 1)
    first = lane < HEAD_DIM
    for p in range(model_width // pair):
        cols = slice(p * pair, (p + 1) * pair)
        q2 = q_ref[:, cols]
        k2 = kv_ref[:, cols]
        v2 = kv_ref[:, model_width + p * pair : model_width + (p + 1) * pair]
        ga2 = ga_ref[:, cols]
        outs = []
        for j in range(2):
            side = first if j == 0 else jnp.logical_not(first)
            qj = jnp.where(side, q2, jnp.zeros_like(q2))
            gaj = jnp.where(side, ga2, jnp.zeros_like(ga2))
            scores = lax.dot_general(qj, k2, (((1,), (1,)), ((), ())), preferred_element_type=F32) * scale
            unnormed = jnp.where(keep, jnp.exp(scores), 0.0)
            denominator = jnp.sum(unnormed, axis=1, keepdims=True) + empty
            attention = (unnormed / denominator).astype(BF16)
            attended = jnp.dot(attention, v2, preferred_element_type=F32)
            weights = lax.dot_general(gaj, v2, (((1,), (1,)), ((), ())), preferred_element_type=F32)
            wide = attention.astype(F32)
            inner = jnp.sum(wide * weights, axis=1, keepdims=True)
            grad_scores = (wide * (weights - inner) * scale).astype(BF16)
            gq = jnp.dot(grad_scores, k2, preferred_element_type=F32)
            gk = jnp.dot(grad_scores.T, qj, preferred_element_type=F32)
            gv = jnp.dot(attention.T, gaj, preferred_element_type=F32)
            outs.append((attended, gq, gk, gv))
        (a0, q0, k0, v0), (a1, q1, k1, v1) = outs
        att_ref[:, cols] = (jnp.where(first, a0, a1) * valid).astype(att_ref.dtype)
        gq_ref[:, cols] = jnp.where(first, q0, q1).astype(gq_ref.dtype)
        gkv_ref[:, cols] = jnp.where(first, k0, k1)
        gkv_ref[:, model_width + p * pair : model_width + (p + 1) * pair] = jnp.where(first, v0, v1)


def attention(queries, grid, grad_attended, token_key_mask, token_valid):
    tokens, model_width = queries.shape
    keys = grid.shape[0]
    whole = pl.BlockSpec(memory_space=pltpu.VMEM)
    flops = 2 * 2 * tokens * keys * 2 * model_width * 5
    return pl.pallas_call(
        attention_kernel,
        out_shape=(
            jax.ShapeDtypeStruct((tokens, model_width), BF16),
            jax.ShapeDtypeStruct((tokens, model_width), BF16),
            jax.ShapeDtypeStruct((keys, 2 * model_width), F32),
        ),
        in_specs=[whole] * 5,
        out_specs=(whole, whole, whole),
        compiler_params=pltpu.CompilerParams(vmem_limit_bytes=48 * 1024 * 1024),
        cost_estimate=pl.CostEstimate(flops=flops, transcendentals=2 * tokens * keys * model_width // HEAD_DIM, bytes_accessed=12 * 1024 * 1024),
    )(queries, grid, grad_attended, token_key_mask, token_valid)


def local(latent, norm_shift, norm_scale, branch_gate, query_key_value, output_weight, tile_valid, cotangent):
    _, height, across, model_width = latent.shape
    tile_rows, tile_cols = height // TILE, across // TILE
    tiles = tile_rows * tile_cols
    tokens = tiles * CELLS
    heads = model_width // HEAD_DIM
    grid_tiles = (tile_rows + 2) * (tile_cols + 2)

    mask_whole = jnp.pad(tile_valid[0].astype(F32), ((1, 1), (1, 1)))
    row_start = lax.axis_index("row") * tile_rows
    col_start = lax.axis_index("col") * tile_cols
    mask_pad = lax.dynamic_slice(mask_whole, (row_start, col_start), (tile_rows + 2, tile_cols + 2))
    key_mask = jnp.asarray(neighbour_table(tile_rows, tile_cols)) * mask_pad.reshape(1, grid_tiles)
    token_key_mask = jnp.repeat(jnp.repeat(key_mask, CELLS, axis=0), CELLS, axis=1)
    query_valid = mask_pad[1:-1, 1:-1].reshape(tiles)
    token_valid = jnp.repeat(query_valid, CELLS)[:, None]

    image = to_tiles(latent[0])
    incoming = to_tiles(cotangent[0]).astype(F32)
    values = image.astype(F32)
    center = values - jnp.mean(values, axis=-1, keepdims=True)
    inverse = lax.rsqrt(jnp.mean(center * center, axis=-1, keepdims=True) + EPSILON)
    normed = center * inverse
    scale_one = 1.0 + norm_scale
    modulated = (normed * scale_one + norm_shift).astype(BF16)
    projections = jnp.dot(modulated, query_key_value, preferred_element_type=F32).astype(BF16)

    queries = projections[:, :model_width]
    key_value = projections[:, model_width:].reshape(tile_rows, tile_cols, CELLS, 2 * model_width)
    grid = halo(key_value).reshape(grid_tiles * CELLS, 2 * model_width)

    grad_projected = (incoming * branch_gate).astype(BF16)
    grad_image = jnp.einsum("nf,df->nd", grad_projected, output_weight, preferred_element_type=F32)
    grad_attended = (grad_image * token_valid).astype(BF16)
    attended, grad_q, pair_grid = attention(queries, grid, grad_attended, token_key_mask, token_valid)

    projected = jnp.dot(attended, output_weight, preferred_element_type=F32)
    gate_term = jnp.sum(incoming * projected, axis=0)
    output_term = jnp.einsum("nd,nf->df", attended, grad_projected, preferred_element_type=F32)
    pair_grid = pair_grid.reshape(tile_rows + 2, tile_cols + 2, CELLS, 2 * model_width)
    pair_grads = return_rims(pair_grid).reshape(tokens, 2 * model_width)

    grad_all = jnp.concatenate([grad_q, pair_grads.astype(BF16)], axis=-1)
    input_term = jnp.einsum("nd,nf->df", modulated, grad_all, preferred_element_type=F32)
    grad_modulated = jnp.einsum("nf,df->nd", grad_all, query_key_value, preferred_element_type=F32)
    shift_term = jnp.sum(grad_modulated, axis=0)
    scale_term = jnp.sum(grad_modulated * normed, axis=0)
    grad_normed = grad_modulated * scale_one
    latent_term = inverse * (
        grad_normed
        - jnp.mean(grad_normed, axis=-1, keepdims=True)
        - normed * jnp.mean(grad_normed * normed, axis=-1, keepdims=True)
    )

    mixed = (values + branch_gate * projected).astype(BF16)
    latent_grad = (incoming + latent_term).astype(BF16)

    output_grad, _ = reduce_weights(output_term, None, on_permutes=True)
    input_grad, sums = reduce_weights(input_term, jnp.stack([shift_term, scale_term, gate_term]))

    return (
        from_tiles(mixed, height, across)[None],
        from_tiles(latent_grad, height, across)[None],
        input_grad,
        output_grad,
        sums[0:1],
        sums[1:2],
        sums[2:3],
    )


def solution(mesh):
    placed = (
        P("dp", "row", "col", None),
        P("dp", None),
        P("dp", None),
        P("dp", None),
        P(),
        P(),
        P("dp", None, None),
        P("dp", "row", "col", None),
    )
    return jax.shard_map(
        local,
        mesh=mesh,
        in_specs=placed,
        out_specs=(
            P("dp", "row", "col", None),
            P("dp", "row", "col", None),
            P("dp", ("row", "col")),
            P("dp", ("row", "col")),
            P("dp", None),
            P("dp", None),
            P("dp", None),
        ),
        check_vma=False,
    )
```
